512 devices in a mesh: lat: 16 (over y, x), lon: 32 (over z, core).
Axes of the slice: x: 4, y: 4, z: 16, core: 2. Of those that a mesh axis runs over, the one named last changes fastest.
Arguments:
- cotangent: bfloat16 [144, 32, 4096], P(None, 'lat', 'lon'), may hold values from -4.5 to 6.5
- cell_area: float32 [32, 4096], P('lat', 'lon'), may hold values from 0.01 to 4
- reach_count: int32 [16, 32], P('lat', 'lon'), may hold values from 1 to 8, as said below
- weights: bfloat16 [16, 32, 8, 256, 768], P('lat', 'lon'), may hold values from -0.0625 to 0.0625
Outputs:
- tracer_adjoint: float32 [144, 32, 4096], P(None, 'lat', 'lon')
The draws below stay inside these ranges and needn't reach their ends.
Inputs may be any that keep to these rules, and one draw needn't show every extreme that they name: reach_count[l, n] counts the tiles (l, n), (l, n - 1), ... (column index modulo 32) that the departure regions of tile (l, n) touch; in every draw one whole latitude row of tiles has 8.
All inputs are finite; a program needn't handle non-finite values.
Results may differ from the reference program's by a relative error of at most 0.0027.
Values may be sent and summed in bfloat16 or wider, within the bound.
No kernel may reach another device: no remote copies, remote signals or barrier semaphores. Data moves between devices by JAX's collectives and lax.ppermute only.
A program may use at most 64 MiB of HBM per device.

```python
import math
import jax
import jax.numpy as jnp
from jax import lax

FIELDS = 144
SLOTS = 8
CELLS = 256
LAT_TILES = 16
LON_TILES = 32
GRID_ROWS = 32
GRID_COLS = 4096


def draw_cotangent(key, part):
    field_shape = (FIELDS, GRID_ROWS, GRID_COLS)
    values = 0.6 + jnp.clip(jax.random.normal(key, field_shape), -4.0, 4.0)
    return values.astype(jnp.float32).astype(jnp.bfloat16)


def draw_cell_area(key, part):
    key_row, key_col, key_cell = jax.random.split(key, 3)
    row_rise = 1.0 + 2.0 * jnp.arange(GRID_ROWS, dtype=jnp.float32)[:, None] / GRID_ROWS
    row_scale = jnp.exp(jax.random.uniform(key_row, (GRID_ROWS, 1)) * math.log(4.0))
    col_scale = jnp.exp(jax.random.uniform(key_col, (1, GRID_COLS)) * math.log(10.0))
    cell_rough = jax.random.uniform(key_cell, (GRID_ROWS, GRID_COLS), minval=0.7, maxval=1.3)
    return (0.02 * row_rise * row_scale * col_scale * cell_rough).astype(jnp.float32)


def draw_reach_count(key, part):
    key_jet, key_fill = jax.random.split(key)
    jet_row = jax.random.randint(key_jet, (), 0, LAT_TILES)
    distance = jnp.abs(jnp.arange(LAT_TILES, dtype=jnp.int32)[:, None] - jet_row)
    highest = jnp.maximum(1, SLOTS - 2 * distance)
    lowest = jnp.maximum(1, highest // 2)
    spread = jax.random.randint(key_fill, (LAT_TILES, LON_TILES), 0, 1048576)
    counts = lowest + spread % (highest - lowest + 1)
    return jnp.where(distance == 0, SLOTS, counts).astype(jnp.int32)


def shard_levels(stream_key, shape, cuts, least, top_value):
    level, own = 1.0, jax.random.fold_in(stream_key, 6)
    for position, shards_of in cuts:
        draws = jnp.exp(jax.random.uniform(jax.random.fold_in(own, position), (shards_of,), jnp.float32, least / len(cuts), top_value / len(cuts)))
        level = level * jnp.repeat(draws, shape[position] // shards_of).reshape([-1 if axis == position else 1 for axis in range(len(shape))])
    return level


def centred(stream_key, dims, width, reach, pieces=(), held_as=jnp.bfloat16):
    loudness = shard_levels(stream_key, dims, pieces, -0.22, 0.18) if pieces else 1.0
    array = jax.random.normal(stream_key, dims, jnp.float32) * width * loudness
    return jnp.minimum(jnp.maximum(array, -reach), reach).astype(held_as)


def setup_inputs(seed: int = 0) -> dict:
    key_list = jax.random.split(jax.random.key(seed), 5)
    cotangent = draw_cotangent(jax.random.fold_in(key_list[4], 71), 0)
    cell_area = draw_cell_area(jax.random.fold_in(key_list[4], 71), 0)
    reach_count = draw_reach_count(jax.random.fold_in(key_list[4], 71), 0)
    weights = centred(key_list[3], (LAT_TILES, LON_TILES, SLOTS, CELLS, 3 * CELLS), (32 * CELLS) ** -0.5, 0.0625, ((0, 16), (1, 32)))
    return {"cotangent": cotangent, "cell_area": cell_area, "reach_count": reach_count, "weights": weights}


def reference(cotangent, cell_area, reach_count, weights):
    fields, grid_rows, grid_cols = cotangent.shape
    lat_tiles, lon_tiles, slot_count, cell_count, moment_cols = weights.shape
    tile_rows = grid_rows // lat_tiles
    tile_cols = grid_cols // lon_tiles
    cot_full = cotangent.astype(jnp.float32)
    factor = jnp.sum(cot_full * cell_area[None], axis=(1, 2)) / jnp.sum(cell_area * cell_area)
    correction = cell_area[None] * factor[:, None, None]
    adjoint_flux = (cot_full - correction).astype(jnp.bfloat16)
    tiles = adjoint_flux.reshape(fields, lat_tiles, tile_rows, lon_tiles, tile_cols)
    tiles = tiles.transpose(1, 3, 0, 2, 4).reshape(lat_tiles, lon_tiles, fields, cell_count)

    def one_row(packed):
        row_tiles, row_weights, row_count = packed
        running = jnp.zeros((lon_tiles, fields, moment_cols), jnp.float32)
        for slot_index in range(slot_count):
            moved_flux = jnp.roll(row_tiles, -slot_index, axis=0)
            moved_count = jnp.roll(row_count, -slot_index, axis=0)
            product = jnp.einsum('nkc,ncd->nkd', moved_flux.astype(jnp.float32), row_weights[:, slot_index].astype(jnp.float32))
            running = running + jnp.where((moved_count > slot_index)[:, None, None], product, 0.0)
        return running

    moments = lax.map(one_row, (tiles, weights, reach_count))
    moments = moments.reshape(lat_tiles, lon_tiles, fields, 3, tile_rows, tile_cols)
    moments = moments.transpose(2, 3, 0, 4, 1, 5).reshape(fields, 3, grid_rows, grid_cols)
    mean_adj = moments[:, 0]
    slope_adj = moments[:, 1]
    curv_adj = moments[:, 2]
    left_sum = slope_adj - 3.0 * curv_adj
    right_sum = slope_adj + 3.0 * curv_adj
    near = left_sum + jnp.roll(left_sum, 1, axis=-1) - right_sum - jnp.roll(right_sum, -1, axis=-1)
    far = jnp.roll(left_sum, -1, axis=-1) + jnp.roll(left_sum, 2, axis=-1) - jnp.roll(right_sum, -2, axis=-1) - jnp.roll(right_sum, 1, axis=-1)
    return mean_adj + 6.0 * curv_adj + (7.0 / 12.0) * near - (1.0 / 12.0) * far + correction
```

```python
import jax
import jax.numpy as jnp
from jax import lax
from jax.sharding import PartitionSpec as P


def shifted(value, axis, by):
    length = lax.axis_size(axis)
    return lax.ppermute(value, axis, [(i, (i + by) % length) for i in range(length)])


def butterfly_sum(value, axes):
    for axis in axes:
        length = lax.axis_size(axis)
        step = 1
        while step < length:
            value = value + lax.ppermute(value, axis, [(i, i ^ step) for i in range(length)])
            step *= 2
    return value


def padded_2(block, sides, width):
    for axis, dim in sides:
        count = lax.axis_size(axis)
        forward = [(i, i + 1) for i in range(count - 1)]
        forward.append((count - 1, 0))
        backward = [(target, source) for source, target in forward]
        low = lax.ppermute(
            lax.slice_in_dim(block, block.shape[dim] - width, None, axis=dim), axis, forward
        )
        high = lax.ppermute(lax.slice_in_dim(block, 0, width, axis=dim), axis, backward)
        block = jnp.concatenate([low, block, high], axis=dim)
    return block


def split_bf16(value):
    high = lax.reduce_precision(value, exponent_bits=8, mantissa_bits=7)
    rest = value - high
    middle = lax.reduce_precision(rest, exponent_bits=8, mantissa_bits=7)
    low = rest - middle
    return [part.astype(jnp.bfloat16) for part in (high, middle, low)]


def on_device(cotangent, cell_area, reach_count, weights):
    fields, tile_rows, tile_cols = cotangent.shape
    cell_count = tile_rows * tile_cols
    slot_count = weights.shape[2]
    cot_full = cotangent.astype(jnp.float32)
    weighted = jnp.sum(cot_full * cell_area[None], axis=(1, 2))
    squares = jnp.sum(cell_area * cell_area)
    stats = butterfly_sum(jnp.concatenate([weighted, squares[None]]), ("lat", "lon"))
    factor = stats[:fields] / stats[fields]

    area_parts = split_bf16(cell_area.reshape(1, cell_count))
    payload = jnp.concatenate([cotangent.reshape(fields, cell_count)] + area_parts, axis=0)
    count_here = reach_count[0, 0]
    tiles = []
    for slot_index in range(slot_count):
        live = jnp.where(count_here > slot_index, payload, jnp.zeros_like(payload))
        tiles.append(live if slot_index == 0 else shifted(live, "lon", -slot_index))
    stacked = jnp.stack(tiles)
    moments = lax.dot_general(
        stacked, weights[0, 0], (((0, 2), (0, 1)), ((), ())), preferred_element_type=jnp.float32
    )
    area_moments = moments[fields] + moments[fields + 1] + moments[fields + 2]
    moments = jnp.concatenate([moments[:fields], area_moments[None]], axis=0)
    moments = moments.reshape(fields + 1, 3, tile_rows, tile_cols)
    mean_adj = moments[:, 0]
    curv_adj = moments[:, 2]
    signs = jnp.array([-3.0, 3.0], jnp.float32)[None, :, None, None]
    edge_pair = moments[:, 1:2] + signs * moments[:, 2:3]
    padded = padded_2(edge_pair, (("lon", 3),), 2)
    left_pad = padded[:, 0]
    right_pad = padded[:, 1]
    near = (
        left_pad[..., 2 : tile_cols + 2]
        + left_pad[..., 1 : tile_cols + 1]
        - right_pad[..., 2 : tile_cols + 2]
        - right_pad[..., 3 : tile_cols + 3]
    )
    far = (
        left_pad[..., 3 : tile_cols + 3]
        + left_pad[..., 0:tile_cols]
        - right_pad[..., 4 : tile_cols + 4]
        - right_pad[..., 1 : tile_cols + 1]
    )
    stencil = mean_adj + 6.0 * curv_adj + 7.0 / 12.0 * near - 1.0 / 12.0 * far
    return stencil[:fields] + factor[:, None, None] * (cell_area[None] - stencil[fields][None])


def solution(mesh):
    in_specs = (
        P(None, "lat", "lon"),
        P("lat", "lon"),
        P("lat", "lon"),
        P("lat", "lon", None, None, None),
    )
    out_specs = P(None, "lat", "lon")
    return jax.shard_map(
        on_device, mesh=mesh, in_specs=in_specs, out_specs=out_specs, check_vma=False
    )
```

```python
import jax
import jax.numpy as jnp
from jax import lax
from jax.sharding import PartitionSpec as P


def shifted(value, axis, by):
    length = lax.axis_size(axis)
    return lax.ppermute(value, axis, [(i, (i + by) % length) for i in range(length)])


def butterfly_sum(value, axes):
    for axis in axes:
        length = lax.axis_size(axis)
        step = 1
        while step < length:
            value = value + lax.ppermute(value, axis, [(i, i ^ step) for i in range(length)])
            step *= 2
    return value


def padded_2(block, sides, width):
    for axis, dim in sides:
        count = lax.axis_size(axis)
        forward = [(i, i + 1) for i in range(count - 1)]
        forward.append((count - 1, 0))
        backward = [(target, source) for source, target in forward]
        low = lax.ppermute(
            lax.slice_in_dim(block, block.shape[dim] - width, None, axis=dim), axis, forward
        )
        high = lax.ppermute(lax.slice_in_dim(block, 0, width, axis=dim), axis, backward)
        block = jnp.concatenate([low, block, high], axis=dim)
    return block


def split_bf16(value):
    high = lax.reduce_precision(value, exponent_bits=8, mantissa_bits=7)
    rest = value - high
    middle = lax.reduce_precision(rest, exponent_bits=8, mantissa_bits=7)
    low = rest - middle
    return [part.astype(jnp.bfloat16) for part in (high, middle, low)]


def on_device(cotangent, cell_area, reach_count, weights):
    fields, tile_rows, tile_cols = cotangent.shape
    cell_count = tile_rows * tile_cols
    slot_count = weights.shape[2]
    cot_full = cotangent.astype(jnp.float32)
    weighted = jnp.sum(cot_full * cell_area[None], axis=(1, 2))
    squares = jnp.sum(cell_area * cell_area)
    stats = butterfly_sum(jnp.concatenate([weighted, squares[None]]), ("lat", "lon"))
    factor = stats[:fields] / stats[fields]

    area_parts = split_bf16(cell_area.reshape(1, cell_count))
    count_row = jnp.full((1, cell_count), reach_count[0, 0], jnp.float32).astype(jnp.bfloat16)
    payload = jnp.concatenate([cotangent.reshape(fields, cell_count)] + area_parts + [count_row], axis=0)
    ring = [payload]
    for _ in range(slot_count // 2):
        ring.append(shifted(ring[-1], "lon", -2))
    odd = lax.axis_index("lon") % 2 == 1
    half = slot_count // 2
    offer = jnp.where(odd, jnp.stack(ring[:half]), jnp.stack(ring[1 : half + 1]))
    swapped = lax.ppermute(offer, "lon", [(i, i ^ 1) for i in range(lax.axis_size("lon"))])
    tiles = []
    for slot_index in range(slot_count):
        tile = ring[slot_index // 2] if slot_index % 2 == 0 else swapped[slot_index // 2]
        live = tile[fields + 3, 0].astype(jnp.float32) > slot_index
        tiles.append(jnp.where(live, tile[: fields + 3], jnp.zeros_like(tile[: fields + 3])))
    stacked = jnp.stack(tiles)
    moments = lax.dot_general(
        stacked, weights[0, 0], (((0, 2), (0, 1)), ((), ())), preferred_element_type=jnp.float32
    )
    area_moments = moments[fields] + moments[fields + 1] + moments[fields + 2]
    moments = jnp.concatenate([moments[:fields], area_moments[None]], axis=0)
    moments = moments.reshape(fields + 1, 3, tile_rows, tile_cols)
    mean_adj = moments[:, 0]
    curv_adj = moments[:, 2]
    signs = jnp.array([-3.0, 3.0], jnp.float32)[None, :, None, None]
    edge_pair = moments[:, 1:2] + signs * moments[:, 2:3]
    padded = padded_2(edge_pair, (("lon", 3),), 2)
    left_pad = padded[:, 0]
    right_pad = padded[:, 1]
    near = (
        left_pad[..., 2 : tile_cols + 2]
        + left_pad[..., 1 : tile_cols + 1]
        - right_pad[..., 2 : tile_cols + 2]
        - right_pad[..., 3 : tile_cols + 3]
    )
    far = (
        left_pad[..., 3 : tile_cols + 3]
        + left_pad[..., 0:tile_cols]
        - right_pad[..., 4 : tile_cols + 4]
        - right_pad[..., 1 : tile_cols + 1]
    )
    stencil = mean_adj + 6.0 * curv_adj + 7.0 / 12.0 * near - 1.0 / 12.0 * far
    return stencil[:fields] + factor[:, None, None] * (cell_area[None] - stencil[fields][None])


def solution(mesh):
    in_specs = (
        P(None, "lat", "lon"),
        P("lat", "lon"),
        P("lat", "lon"),
        P("lat", "lon", None, None, None),
    )
    out_specs = P(None, "lat", "lon")
    return jax.shard_map(
        on_device, mesh=mesh, in_specs=in_specs, out_specs=out_specs, check_vma=False
    )
```

```python
import jax
import jax.numpy as jnp
from jax import lax
from jax.sharding import PartitionSpec as P


def shifted(value, axis, by):
    length = lax.axis_size(axis)
    return lax.ppermute(value, axis, [(i, (i + by) % length) for i in range(length)])


def butterfly_sum(value, axes):
    for axis in axes:
        length = lax.axis_size(axis)
        step = 1
        while step < length:
            partner = lax.ppermute(value, axis, [(i, i ^ step) for i in range(length)])
            value = value + partner
            step *= 2
    return value


def padded_2(block, sides, width):
    for axis, dim in sides:
        count = lax.axis_size(axis)
        forward = [(i, i + 1) for i in range(count - 1)]
        forward.append((count - 1, 0))
        backward = [(target, source) for source, target in forward]
        low = lax.ppermute(
            lax.slice_in_dim(block, block.shape[dim] - width, None, axis=dim), axis, forward
        )
        high = lax.ppermute(lax.slice_in_dim(block, 0, width, axis=dim), axis, backward)
        block = jnp.concatenate([low, block, high], axis=dim)
    return block


def split_bf16(value):
    high = lax.reduce_precision(value, exponent_bits=8, mantissa_bits=7)
    rest = value - high
    middle = lax.reduce_precision(rest, exponent_bits=8, mantissa_bits=7)
    low = rest - middle
    return [part.astype(jnp.bfloat16) for part in (high, middle, low)]


def on_device_body(cotangent, cell_area, reach_count, weights):
    fields, tile_rows, tile_cols = cotangent.shape
    cell_count = tile_rows * tile_cols
    slot_count = weights.shape[2]
    cot_full = cotangent.astype(jnp.float32)
    weighted = jnp.sum(cot_full * cell_area[None], axis=(1, 2))
    squares = jnp.sum(cell_area * cell_area)
    stats = butterfly_sum(jnp.concatenate([weighted, squares[None]]), ("lat", "lon"))
    factor = stats[:fields] / stats[fields]

    area_parts = split_bf16(cell_area.reshape(1, cell_count))
    count_row = jnp.full((1, cell_count), reach_count[0, 0], jnp.float32).astype(jnp.bfloat16)
    payload = jnp.concatenate([cotangent.reshape(fields, cell_count)] + area_parts + [count_row], axis=0)
    ring = [payload]
    for _ in range(slot_count // 2):
        ring.append(shifted(ring[-1], "lon", -2))
    odd = lax.axis_index("lon") % 2 == 1
    half = slot_count // 2
    offer = jnp.where(odd, jnp.stack(ring[:half]), jnp.stack(ring[1 : half + 1]))
    swapped = lax.ppermute(offer, "lon", [(i, i ^ 1) for i in range(lax.axis_size("lon"))])
    tiles = []
    for slot_index in range(slot_count):
        tile = ring[slot_index // 2] if slot_index % 2 == 0 else swapped[slot_index // 2]
        live = tile[fields + 3, 0].astype(jnp.float32) > slot_index
        tiles.append(jnp.where(live, tile[: fields + 3], jnp.zeros_like(tile[: fields + 3])))
    stacked = jnp.stack(tiles)
    moments = lax.dot_general(
        stacked, weights[0, 0], (((0, 2), (0, 1)), ((), ())), preferred_element_type=jnp.float32
    )
    area_moments = moments[fields] + moments[fields + 1] + moments[fields + 2]
    moments = jnp.concatenate([moments[:fields], area_moments[None]], axis=0)
    moments = moments.reshape(fields + 1, 3, tile_rows, tile_cols)
    mean_adj = moments[:, 0]
    curv_adj = moments[:, 2]
    signs = jnp.array([-3.0, 3.0], jnp.float32)[None, :, None, None]
    edge_pair = moments[:, 1:2] + signs * moments[:, 2:3]
    padded = padded_2(edge_pair, (("lon", 3),), 2)
    left_pad = padded[:, 0]
    right_pad = padded[:, 1]
    near = (
        left_pad[..., 2 : tile_cols + 2]
        + left_pad[..., 1 : tile_cols + 1]
        - right_pad[..., 2 : tile_cols + 2]
        - right_pad[..., 3 : tile_cols + 3]
    )
    far = (
        left_pad[..., 3 : tile_cols + 3]
        + left_pad[..., 0:tile_cols]
        - right_pad[..., 4 : tile_cols + 4]
        - right_pad[..., 1 : tile_cols + 1]
    )
    stencil = mean_adj + 6.0 * curv_adj + 7.0 / 12.0 * near - 1.0 / 12.0 * far
    return stencil[:fields] + factor[:, None, None] * (cell_area[None] - stencil[fields][None])


def solution(mesh):
    in_specs = (
        P(None, "lat", "lon"),
        P("lat", "lon"),
        P("lat", "lon"),
        P("lat", "lon", None, None, None),
    )
    out_specs = P(None, "lat", "lon")
    return jax.shard_map(
        on_device_body, mesh=mesh, in_specs=in_specs, out_specs=out_specs, check_vma=False
    )
```

```python
import jax
import jax.numpy as jnp
from jax import lax
from jax.sharding import PartitionSpec as P


def shifted(value, axis, by):
    length = lax.axis_size(axis)
    return lax.ppermute(value, axis, [(i, (i + by) % length) for i in range(length)])


def butterfly_sum(value, axes):
    for axis in axes:
        length = lax.axis_size(axis)
        step = 1
        while step < length:
            partner = lax.ppermute(value, axis, [(i, i ^ step) for i in range(length)])
            value = value + partner
            step *= 2
    return value


def padded_2(block, sides, width):
    for axis, dim in sides:
        count = lax.axis_size(axis)
        forward = [(i, i + 1) for i in range(count - 1)]
        forward.append((count - 1, 0))
        backward = [(target, source) for source, target in forward]
        low = lax.ppermute(
            lax.slice_in_dim(block, block.shape[dim] - width, None, axis=dim), axis, forward
        )
        high = lax.ppermute(lax.slice_in_dim(block, 0, width, axis=dim), axis, backward)
        block = jnp.concatenate([low, block, high], axis=dim)
    return block


def split_bf16(value):
    high = lax.reduce_precision(value, exponent_bits=8, mantissa_bits=7)
    rest = value - high
    middle = lax.reduce_precision(rest, exponent_bits=8, mantissa_bits=7)
    low = rest - middle
    return [part.astype(jnp.bfloat16) for part in (high, middle, low)]


def on_device_body(cotangent, cell_area, reach_count, weights):
    fields, tile_rows, tile_cols = cotangent.shape
    cell_count = tile_rows * tile_cols
    slot_count = weights.shape[2]
    cot_full = cotangent.astype(jnp.float32)
    weighted = jnp.sum(cot_full * cell_area[None], axis=(1, 2))
    squares = jnp.sum(cell_area * cell_area)
    stats, area_late = lax.optimization_barrier((jnp.concatenate([weighted, squares[None]]), cell_area))
    stats = butterfly_sum(stats, ("lat", "lon"))
    factor = stats[:fields] / stats[fields]

    area_parts = split_bf16(cell_area.reshape(1, cell_count))
    count_row = jnp.full((1, cell_count), reach_count[0, 0], jnp.float32).astype(jnp.bfloat16)
    payload = jnp.concatenate([cotangent.reshape(fields, cell_count)] + area_parts + [count_row], axis=0)
    payload = lax.optimization_barrier(payload)
    ring = [payload]
    for _ in range(slot_count // 2):
        ring.append(shifted(ring[-1], "lon", -2))
    odd = lax.axis_index("lon") % 2 == 1
    half = slot_count // 2
    offer = jnp.stack([jnp.where(odd, ring[k], ring[k + 1]) for k in range(half)])
    offer = lax.optimization_barrier(offer)
    swapped = lax.ppermute(offer, "lon", [(i, i ^ 1) for i in range(lax.axis_size("lon"))])
    pairs = jnp.stack([jnp.stack(ring[:half]), swapped], axis=1)
    stacked = pairs.reshape(slot_count, fields + 4, cell_count)
    counts = stacked[:, fields + 3, 0].astype(jnp.float32)
    live = counts > jnp.arange(slot_count, dtype=jnp.float32)
    stacked = jnp.where(live[:, None, None], stacked, jnp.zeros_like(stacked))
    moments = lax.dot_general(
        stacked, weights[0, 0], (((0, 2), (0, 1)), ((), ())), preferred_element_type=jnp.float32
    )
    moments = moments.reshape(fields + 4, 3, tile_rows, tile_cols)
    mean_adj = moments[:, 0]
    curv_adj = moments[:, 2]
    signs = jnp.array([-3.0, 3.0], jnp.float32)[None, :, None, None]
    edge_pair = moments[:, 1:2] + signs * moments[:, 2:3]
    padded = padded_2(edge_pair, (("lon", 3),), 2)
    left_pad = padded[:, 0]
    right_pad = padded[:, 1]
    near = (
        left_pad[..., 2 : tile_cols + 2]
        + left_pad[..., 1 : tile_cols + 1]
        - right_pad[..., 2 : tile_cols + 2]
        - right_pad[..., 3 : tile_cols + 3]
    )
    far = (
        left_pad[..., 3 : tile_cols + 3]
        + left_pad[..., 0:tile_cols]
        - right_pad[..., 4 : tile_cols + 4]
        - right_pad[..., 1 : tile_cols + 1]
    )
    stencil = mean_adj + 6.0 * curv_adj + 7.0 / 12.0 * near - 1.0 / 12.0 * far
    area_stencil = stencil[fields] + stencil[fields + 1] + stencil[fields + 2]
    return stencil[:fields] + factor[:, None, None] * (area_late[None] - area_stencil[None])


def solution(mesh):
    in_specs = (
        P(None, "lat", "lon"),
        P("lat", "lon"),
        P("lat", "lon"),
        P("lat", "lon", None, None, None),
    )
    out_specs = P(None, "lat", "lon")
    return jax.shard_map(
        on_device_body, mesh=mesh, in_specs=in_specs, out_specs=out_specs, check_vma=False
    )
```

```python
import jax
import jax.numpy as jnp
from jax import lax
from jax.sharding import PartitionSpec as P


def shifted(value, axis, by):
    length = lax.axis_size(axis)
    return lax.ppermute(value, axis, [(i, (i + by) % length) for i in range(length)])


def butterfly_sum(value, axes):
    for axis in axes:
        length = lax.axis_size(axis)
        step = 1
        while step < length:
            partner = lax.ppermute(value, axis, [(i, i ^ step) for i in range(length)])
            value = value + partner
            step *= 2
    return value


def padded_2(block, sides, width):
    for axis, dim in sides:
        count = lax.axis_size(axis)
        forward = [(i, i + 1) for i in range(count - 1)]
        forward.append((count - 1, 0))
        backward = [(target, source) for source, target in forward]
        low = lax.ppermute(
            lax.slice_in_dim(block, block.shape[dim] - width, None, axis=dim), axis, forward
        )
        high = lax.ppermute(lax.slice_in_dim(block, 0, width, axis=dim), axis, backward)
        block = jnp.concatenate([low, block, high], axis=dim)
    return block


def split_bf16(value):
    high = lax.reduce_precision(value, exponent_bits=8, mantissa_bits=7)
    rest = value - high
    middle = lax.reduce_precision(rest, exponent_bits=8, mantissa_bits=7)
    low = rest - middle
    return [part.astype(jnp.bfloat16) for part in (high, middle, low)]


def on_device_body(cotangent, cell_area, reach_count, weights):
    fields, tile_rows, tile_cols = cotangent.shape
    cell_count = tile_rows * tile_cols
    slot_count = weights.shape[2]
    cot_full = cotangent.astype(jnp.float32)
    weighted = jnp.sum(cot_full * cell_area[None], axis=(1, 2))
    squares = jnp.sum(cell_area * cell_area)
    stats, area_late = lax.optimization_barrier((jnp.concatenate([weighted, squares[None]]), cell_area))
    stats = butterfly_sum(stats, ("lat", "lon"))
    factor = stats[:fields] / stats[fields]

    area_parts = split_bf16(cell_area.reshape(1, cell_count))
    count_row = jnp.full((1, cell_count), reach_count[0, 0], jnp.float32).astype(jnp.bfloat16)
    payload = jnp.concatenate([cotangent.reshape(fields, cell_count)] + area_parts + [count_row], axis=0)
    payload = lax.optimization_barrier(payload)
    ring = [payload]
    for _ in range(slot_count // 2):
        ring.append(shifted(ring[-1], "lon", -2))
    odd = lax.axis_index("lon") % 2 == 1
    half = slot_count // 2
    offer = jnp.stack([jnp.where(odd, ring[k], ring[k + 1]) for k in range(half)])
    offer = lax.optimization_barrier(offer)
    swapped = lax.ppermute(offer, "lon", [(i, i ^ 1) for i in range(lax.axis_size("lon"))])
    pairs = jnp.stack([jnp.stack(ring[:half]), swapped], axis=1)
    stacked = pairs.reshape(slot_count, fields + 4, cell_count)
    counts = stacked[:, fields + 3, 0].astype(jnp.float32)
    live = counts > jnp.arange(slot_count, dtype=jnp.float32)
    stacked = jnp.where(live[:, None, None], stacked, jnp.zeros_like(stacked))
    flat = stacked.transpose(1, 0, 2).reshape(fields + 4, slot_count * cell_count)
    moments = jnp.dot(
        flat,
        weights[0, 0].reshape(slot_count * cell_count, 3 * cell_count),
        preferred_element_type=jnp.float32,
    )
    moment = [
        moments[:, m * cell_count : (m + 1) * cell_count].reshape(fields + 4, tile_rows, tile_cols)
        for m in range(3)
    ]
    moments = jnp.stack(moment, axis=1)
    mean_adj = moments[:, 0]
    curv_adj = moments[:, 2]
    signs = jnp.array([-3.0, 3.0], jnp.float32)[None, :, None, None]
    edge_pair = moments[:, 1:2] + signs * moments[:, 2:3]
    padded = padded_2(edge_pair, (("lon", 3),), 2)
    left_pad = padded[:, 0]
    right_pad = padded[:, 1]
    near = (
        left_pad[..., 2 : tile_cols + 2]
        + left_pad[..., 1 : tile_cols + 1]
        - right_pad[..., 2 : tile_cols + 2]
        - right_pad[..., 3 : tile_cols + 3]
    )
    far = (
        left_pad[..., 3 : tile_cols + 3]
        + left_pad[..., 0:tile_cols]
        - right_pad[..., 4 : tile_cols + 4]
        - right_pad[..., 1 : tile_cols + 1]
    )
    stencil = mean_adj + 6.0 * curv_adj + 7.0 / 12.0 * near - 1.0 / 12.0 * far
    area_stencil = stencil[fields] + stencil[fields + 1] + stencil[fields + 2]
    return stencil[:fields] + factor[:, None, None] * (area_late[None] - area_stencil[None])


def solution(mesh):
    in_specs = (
        P(None, "lat", "lon"),
        P("lat", "lon"),
        P("lat", "lon"),
        P("lat", "lon", None, None, None),
    )
    out_specs = P(None, "lat", "lon")
    return jax.shard_map(on_device_body, mesh=mesh, in_specs=in_specs, out_specs=out_specs, check_vma=False)
```

```python
import jax
import jax.numpy as jnp
from jax import lax
from jax.sharding import PartitionSpec as P


def shifted(value, axis, by):
    length = lax.axis_size(axis)
    return lax.ppermute(value, axis, [(i, (i + by) % length) for i in range(length)])


def butterfly_sum(value, axes):
    for axis in axes:
        length = lax.axis_size(axis)
        step = 1
        while step < length:
            partner = lax.ppermute(value, axis, [(i, i ^ step) for i in range(length)])
            value = value + partner
            step *= 2
    return value


def padded_2(block, sides, width):
    for axis, dim in sides:
        count = lax.axis_size(axis)
        forward = [(i, i + 1) for i in range(count - 1)]
        forward.append((count - 1, 0))
        backward = [(target, source) for source, target in forward]
        low = lax.ppermute(
            lax.slice_in_dim(block, block.shape[dim] - width, None, axis=dim), axis, forward
        )
        high = lax.ppermute(lax.slice_in_dim(block, 0, width, axis=dim), axis, backward)
        block = jnp.concatenate([low, block, high], axis=dim)
    return block


def split_bf16(value):
    high = lax.reduce_precision(value, exponent_bits=8, mantissa_bits=7)
    rest = value - high
    middle = lax.reduce_precision(rest, exponent_bits=8, mantissa_bits=7)
    low = rest - middle
    return [part.astype(jnp.bfloat16) for part in (high, middle, low)]


def on_device_body(cotangent, cell_area, reach_count, weights):
    fields, tile_rows, tile_cols = cotangent.shape
    cell_count = tile_rows * tile_cols
    slot_count = weights.shape[2]
    cot_full = cotangent.astype(jnp.float32)
    weighted = jnp.sum(cot_full * cell_area[None], axis=(1, 2))
    squares = jnp.sum(cell_area * cell_area)
    stats, area_late = lax.optimization_barrier((jnp.concatenate([weighted, squares[None]]), cell_area))
    stats = butterfly_sum(stats, ("lat", "lon"))
    factor = stats[:fields] / stats[fields]

    area_parts = split_bf16(cell_area.reshape(1, cell_count))
    count_row = jnp.full((1, cell_count), reach_count[0, 0], jnp.float32).astype(jnp.bfloat16)
    payload = jnp.concatenate([cotangent.reshape(fields, cell_count)] + area_parts + [count_row], axis=0)
    payload = lax.optimization_barrier(payload)
    ring = [payload]
    for _ in range(slot_count // 2):
        ring.append(shifted(ring[-1], "lon", -2))
    odd = lax.axis_index("lon") % 2 == 1
    half = slot_count // 2
    offer = jnp.stack([jnp.where(odd, ring[k], ring[k + 1]) for k in range(half)])
    offer = lax.optimization_barrier(offer)
    swapped = lax.ppermute(offer, "lon", [(i, i ^ 1) for i in range(lax.axis_size("lon"))])
    pairs = jnp.stack([jnp.stack(ring[:half]), swapped], axis=1)
    stacked = pairs.reshape(slot_count, fields + 4, cell_count)
    counts = stacked[:, fields + 3, 0].astype(jnp.float32)
    live = counts > jnp.arange(slot_count, dtype=jnp.float32)
    stacked = jnp.where(live[:, None, None], stacked, jnp.zeros_like(stacked))
    flat = stacked.transpose(1, 0, 2).reshape(fields + 4, slot_count * cell_count)
    moments = jnp.dot(
        flat,
        weights[0, 0].reshape(slot_count * cell_count, 3 * cell_count),
        preferred_element_type=jnp.float32,
    )

    def block(moment_index, row):
        start = moment_index * cell_count + row * tile_cols
        return moments[:, start : start + tile_cols]

    mean_adj = jnp.stack([block(0, row) for row in range(tile_rows)], axis=1)
    curv_adj = jnp.stack([block(2, row) for row in range(tile_rows)], axis=1)
    sides = [
        jnp.stack([block(1, row) + sign * block(2, row) for row in range(tile_rows)], axis=1)
        for sign in (-3.0, 3.0)
    ]
    edge_pair = jnp.stack(sides, axis=1)
    padded = padded_2(edge_pair, (("lon", 3),), 2)
    left_pad = padded[:, 0]
    right_pad = padded[:, 1]
    near = (
        left_pad[..., 2 : tile_cols + 2]
        + left_pad[..., 1 : tile_cols + 1]
        - right_pad[..., 2 : tile_cols + 2]
        - right_pad[..., 3 : tile_cols + 3]
    )
    far = (
        left_pad[..., 3 : tile_cols + 3]
        + left_pad[..., 0:tile_cols]
        - right_pad[..., 4 : tile_cols + 4]
        - right_pad[..., 1 : tile_cols + 1]
    )
    stencil = mean_adj + 6.0 * curv_adj + 7.0 / 12.0 * near - 1.0 / 12.0 * far
    area_stencil = stencil[fields] + stencil[fields + 1] + stencil[fields + 2]
    return stencil[:fields] + factor[:, None, None] * (area_late[None] - area_stencil[None])


def solution(mesh):
    in_specs = (
        P(None, "lat", "lon"),
        P("lat", "lon"),
        P("lat", "lon"),
        P("lat", "lon", None, None, None),
    )
    out_specs = P(None, "lat", "lon")
    return jax.shard_map(
        on_device_body, mesh=mesh, in_specs=in_specs, out_specs=out_specs, check_vma=False
    )
```

```python
import jax
import jax.numpy as jnp
from jax import lax
from jax.sharding import PartitionSpec as P


def shifted(value, axis, by):
    length = lax.axis_size(axis)
    return lax.ppermute(value, axis, [(i, (i + by) % length) for i in range(length)])


def xor_rounds(length):
    rounds, step = [], 1
    while step < length:
        rounds.append([i ^ step for i in range(length)])
        step *= 2
    return rounds


def lat_rounds(length):
    if length != 16:
        return xor_rounds(length)
    def mirror(i, scale):
        digit = (i // scale) % 4
        return i + (3 - 2 * digit) * scale
    return [
        [i ^ 1 for i in range(length)],
        [mirror(i, 1) for i in range(length)],
        [i ^ 4 for i in range(length)],
        [mirror(i, 4) for i in range(length)],
    ]


def lon_rounds(length):
    if length != 32:
        return xor_rounds(length)
    def across(i):
        chip, core = divmod(i, 2)
        return 2 * ((chip + (12 if chip < 4 else 4 if chip < 8 else -4 if chip < 12 else -12)) % 16) + core
    return xor_rounds(length)[:4] + [[across(i) for i in range(length)]]


def butterfly_sum(value, axes):
    for axis in axes:
        length = lax.axis_size(axis)
        for partner_of in (lat_rounds if axis == "lat" else lon_rounds)(length):
            partner = lax.ppermute(value, axis, [(i, partner_of[i]) for i in range(length)])
            value = value + partner
    return value


def padded_2(block, sides, width):
    for axis, dim in sides:
        count = lax.axis_size(axis)
        forward = [(i, i + 1) for i in range(count - 1)]
        forward.append((count - 1, 0))
        backward = [(target, source) for source, target in forward]
        low = lax.ppermute(
            lax.slice_in_dim(block, block.shape[dim] - width, None, axis=dim), axis, forward
        )
        high = lax.ppermute(lax.slice_in_dim(block, 0, width, axis=dim), axis, backward)
        block = jnp.concatenate([low, block, high], axis=dim)
    return block


def split_bf16(value):
    high = lax.reduce_precision(value, exponent_bits=8, mantissa_bits=7)
    rest = value - high
    middle = lax.reduce_precision(rest, exponent_bits=8, mantissa_bits=7)
    low = rest - middle
    return [part.astype(jnp.bfloat16) for part in (high, middle, low)]


def on_device_body(cotangent, cell_area, reach_count, weights):
    fields, tile_rows, tile_cols = cotangent.shape
    cell_count = tile_rows * tile_cols
    slot_count = weights.shape[2]
    cot_full = cotangent.astype(jnp.float32)
    weighted = jnp.sum(cot_full * cell_area[None], axis=(1, 2))
    squares = jnp.sum(cell_area * cell_area)
    stats, area_late = lax.optimization_barrier((jnp.concatenate([weighted, squares[None]]), cell_area))
    stats = butterfly_sum(stats, ("lat", "lon"))
    factor = stats[:fields] / stats[fields]

    area_parts = split_bf16(cell_area.reshape(1, cell_count))
    count_row = jnp.full((1, cell_count), reach_count[0, 0], jnp.float32).astype(jnp.bfloat16)
    payload = jnp.concatenate([cotangent.reshape(fields, cell_count)] + area_parts + [count_row], axis=0)
    payload = lax.optimization_barrier(payload)
    ring = [payload]
    for _ in range(slot_count // 2):
        ring.append(shifted(ring[-1], "lon", -2))
    odd = lax.axis_index("lon") % 2 == 1
    half = slot_count // 2
    offer = jnp.stack([jnp.where(odd, ring[k], ring[k + 1]) for k in range(half)])
    offer = lax.optimization_barrier(offer)
    swapped = lax.ppermute(offer, "lon", [(i, i ^ 1) for i in range(lax.axis_size("lon"))])
    pairs = jnp.stack([jnp.stack(ring[:half]), swapped], axis=1)
    stacked = pairs.reshape(slot_count, fields + 4, cell_count)
    counts = stacked[:, fields + 3, 0].astype(jnp.float32)
    live = counts > jnp.arange(slot_count, dtype=jnp.float32)
    stacked = jnp.where(live[:, None, None], stacked, jnp.zeros_like(stacked))
    flat = stacked.transpose(1, 0, 2).reshape(fields + 4, slot_count * cell_count)
    moments = jnp.dot(
        flat,
        weights[0, 0].reshape(slot_count * cell_count, 3 * cell_count),
        preferred_element_type=jnp.float32,
    )

    def block(moment_index, row):
        start = moment_index * cell_count + row * tile_cols
        return moments[:, start : start + tile_cols]

    mean_adj = jnp.stack([block(0, row) for row in range(tile_rows)], axis=1)
    curv_adj = jnp.stack([block(2, row) for row in range(tile_rows)], axis=1)
    sides = [
        jnp.stack([block(1, row) + sign * block(2, row) for row in range(tile_rows)], axis=1)
        for sign in (-3.0, 3.0)
    ]
    edge_pair = jnp.stack(sides, axis=1)
    padded = padded_2(edge_pair, (("lon", 3),), 2)
    left_pad = padded[:, 0]
    right_pad = padded[:, 1]
    near = (
        left_pad[..., 2 : tile_cols + 2]
        + left_pad[..., 1 : tile_cols + 1]
        - right_pad[..., 2 : tile_cols + 2]
        - right_pad[..., 3 : tile_cols + 3]
    )
    far = (
        left_pad[..., 3 : tile_cols + 3]
        + left_pad[..., 0:tile_cols]
        - right_pad[..., 4 : tile_cols + 4]
        - right_pad[..., 1 : tile_cols + 1]
    )
    stencil = mean_adj + 6.0 * curv_adj + 7.0 / 12.0 * near - 1.0 / 12.0 * far
    area_stencil = stencil[fields] + stencil[fields + 1] + stencil[fields + 2]
    return stencil[:fields] + factor[:, None, None] * (area_late[None] - area_stencil[None])


def solution(mesh):
    in_specs = (
        P(None, "lat", "lon"),
        P("lat", "lon"),
        P("lat", "lon"),
        P("lat", "lon", None, None, None),
    )
    out_specs = P(None, "lat", "lon")
    return jax.shard_map(
        on_device_body, mesh=mesh, in_specs=in_specs, out_specs=out_specs, check_vma=False
    )
```

```python
import jax
import jax.numpy as jnp
from jax import lax
from jax.sharding import PartitionSpec as P


def shifted(value, axis, by):
    length = lax.axis_size(axis)
    return lax.ppermute(value, axis, [(i, (i + by) % length) for i in range(length)])


def xor_rounds(length):
    rounds, step = [], 1
    while step < length:
        rounds.append([i ^ step for i in range(length)])
        step *= 2
    return rounds


def lat_rounds(length):
    if length != 16:
        return xor_rounds(length)
    def mirror(i, scale):
        digit = (i // scale) % 4
        return i + (3 - 2 * digit) * scale
    return [
        [i ^ 1 for i in range(length)],
        [mirror(i, 1) for i in range(length)],
        [i ^ 4 for i in range(length)],
        [mirror(i, 4) for i in range(length)],
    ]


def lon_rounds(length):
    if length != 32:
        return xor_rounds(length)
    def across(i):
        chip, core = divmod(i, 2)
        return 2 * ((chip + (12 if chip < 4 else 4 if chip < 8 else -4 if chip < 12 else -12)) % 16) + core
    return xor_rounds(length)[:4] + [[across(i) for i in range(length)]]


def butterfly_sum(value, axes):
    for axis in axes:
        length = lax.axis_size(axis)
        for partner_of in (lat_rounds if axis == "lat" else lon_rounds)(length):
            partner = lax.ppermute(value, axis, [(i, partner_of[i]) for i in range(length)])
            value = value + partner
    return value


def padded_2(block, sides, width):
    for axis, dim in sides:
        count = lax.axis_size(axis)
        forward = [(i, i + 1) for i in range(count - 1)]
        forward.append((count - 1, 0))
        backward = [(target, source) for source, target in forward]
        low = lax.ppermute(
            lax.slice_in_dim(block, block.shape[dim] - width, None, axis=dim), axis, forward
        )
        high = lax.ppermute(lax.slice_in_dim(block, 0, width, axis=dim), axis, backward)
        block = jnp.concatenate([low, block, high], axis=dim)
    return block


def split_bf16(value):
    high = lax.reduce_precision(value, exponent_bits=8, mantissa_bits=7)
    rest = value - high
    middle = lax.reduce_precision(rest, exponent_bits=8, mantissa_bits=7)
    low = rest - middle
    return [part.astype(jnp.bfloat16) for part in (high, middle, low)]


def on_device_body(cotangent, cell_area, reach_count, weights):
    fields, tile_rows, tile_cols = cotangent.shape
    cell_count = tile_rows * tile_cols
    slot_count = weights.shape[2]
    area_parts = split_bf16(cell_area.reshape(1, cell_count))
    count_row = jnp.full((1, cell_count), reach_count[0, 0], jnp.float32).astype(jnp.bfloat16)
    payload = jnp.concatenate([cotangent.reshape(fields, cell_count)] + area_parts + [count_row], axis=0)
    payload = lax.optimization_barrier(payload)
    products = jnp.dot(
        payload[: fields + 3], jnp.concatenate(area_parts, axis=0).T, preferred_element_type=jnp.float32
    ).sum(axis=1)
    weighted = products[:fields]
    squares = products[fields] + products[fields + 1] + products[fields + 2]
    stats, area_late = lax.optimization_barrier((jnp.concatenate([weighted, squares[None]]), cell_area))
    stats = butterfly_sum(stats, ("lat", "lon"))
    factor = stats[:fields] / stats[fields]

    ring = [payload]
    for _ in range(slot_count // 2):
        ring.append(shifted(ring[-1], "lon", -2))
    odd = lax.axis_index("lon") % 2 == 1
    half = slot_count // 2
    offer = jnp.stack([jnp.where(odd, ring[k], ring[k + 1]) for k in range(half)])
    offer = lax.optimization_barrier(offer)
    swapped = lax.ppermute(offer, "lon", [(i, i ^ 1) for i in range(lax.axis_size("lon"))])
    pairs = jnp.stack([jnp.stack(ring[:half]), swapped], axis=1)
    stacked = pairs.reshape(slot_count, fields + 4, cell_count)
    counts = stacked[:, fields + 3, 0].astype(jnp.float32)
    live = counts > jnp.arange(slot_count, dtype=jnp.float32)
    stacked = jnp.where(live[:, None, None], stacked, jnp.zeros_like(stacked))
    flat = stacked.transpose(1, 0, 2).reshape(fields + 4, slot_count * cell_count)
    moments = jnp.dot(
        flat,
        weights[0, 0].reshape(slot_count * cell_count, 3 * cell_count),
        preferred_element_type=jnp.float32,
    )

    def block(moment_index, row):
        start = moment_index * cell_count + row * tile_cols
        return moments[:, start : start + tile_cols]

    mean_adj = jnp.stack([block(0, row) for row in range(tile_rows)], axis=1)
    curv_adj = jnp.stack([block(2, row) for row in range(tile_rows)], axis=1)
    sides = [
        jnp.stack([block(1, row) + sign * block(2, row) for row in range(tile_rows)], axis=1)
        for sign in (-3.0, 3.0)
    ]
    edge_pair = jnp.stack(sides, axis=1)
    padded = padded_2(edge_pair, (("lon", 3),), 2)
    left_pad = padded[:, 0]
    right_pad = padded[:, 1]
    near = (
        left_pad[..., 2 : tile_cols + 2]
        + left_pad[..., 1 : tile_cols + 1]
        - right_pad[..., 2 : tile_cols + 2]
        - right_pad[..., 3 : tile_cols + 3]
    )
    far = (
        left_pad[..., 3 : tile_cols + 3]
        + left_pad[..., 0:tile_cols]
        - right_pad[..., 4 : tile_cols + 4]
        - right_pad[..., 1 : tile_cols + 1]
    )
    stencil = mean_adj + 6.0 * curv_adj + 7.0 / 12.0 * near - 1.0 / 12.0 * far
    area_stencil = stencil[fields] + stencil[fields + 1] + stencil[fields + 2]
    return stencil[:fields] + factor[:, None, None] * (area_late[None] - area_stencil[None])


def solution(mesh):
    in_specs = (
        P(None, "lat", "lon"),
        P("lat", "lon"),
        P("lat", "lon"),
        P("lat", "lon", None, None, None),
    )
    out_specs = P(None, "lat", "lon")
    return jax.shard_map(on_device_body, mesh=mesh, in_specs=in_specs, out_specs=out_specs, check_vma=False)
```

```python
import jax
import jax.numpy as jnp
from jax import lax
from jax.sharding import PartitionSpec as P


def shifted(value, axis, by):
    length = lax.axis_size(axis)
    return lax.ppermute(value, axis, [(i, (i + by) % length) for i in range(length)])


def xor_rounds(length):
    rounds, step = [], 1
    while step < length:
        rounds.append([i ^ step for i in range(length)])
        step *= 2
    return rounds


def lat_rounds(length):
    if length != 16:
        return xor_rounds(length)
    def mirror(i, scale):
        digit = (i // scale) % 4
        return i + (3 - 2 * digit) * scale
    return [
        [i ^ 1 for i in range(length)],
        [mirror(i, 1) for i in range(length)],
        [i ^ 4 for i in range(length)],
        [mirror(i, 4) for i in range(length)],
    ]


def lon_rounds(length):
    if length != 32:
        return xor_rounds(length)
    def across(i):
        chip, core = divmod(i, 2)
        return 2 * ((chip + (12 if chip < 4 else 4 if chip < 8 else -4 if chip < 12 else -12)) % 16) + core
    return xor_rounds(length)[:4] + [[across(i) for i in range(length)]]


def butterfly_sum(value, axes):
    for axis in axes:
        length = lax.axis_size(axis)
        for partner_of in (lat_rounds if axis == "lat" else lon_rounds)(length):
            partner = lax.ppermute(value, axis, [(i, partner_of[i]) for i in range(length)])
            value = value + partner
    return value


def padded_2(block, sides, width):
    for axis, dim in sides:
        count = lax.axis_size(axis)
        forward = [(i, i + 1) for i in range(count - 1)]
        forward.append((count - 1, 0))
        backward = [(target, source) for source, target in forward]
        low = lax.ppermute(
            lax.slice_in_dim(block, block.shape[dim] - width, None, axis=dim), axis, forward
        )
        high = lax.ppermute(lax.slice_in_dim(block, 0, width, axis=dim), axis, backward)
        block = jnp.concatenate([low, block, high], axis=dim)
    return block


def split_bf16(value):
    high = lax.reduce_precision(value, exponent_bits=8, mantissa_bits=7)
    rest = value - high
    middle = lax.reduce_precision(rest, exponent_bits=8, mantissa_bits=7)
    low = rest - middle
    return [part.astype(jnp.bfloat16) for part in (high, middle, low)]


def on_device_body(cotangent, cell_area, reach_count, weights):
    fields, tile_rows, tile_cols = cotangent.shape
    cell_count = tile_rows * tile_cols
    slot_count = weights.shape[2]
    area_parts = split_bf16(cell_area.reshape(1, cell_count))
    count_row = jnp.full((1, cell_count), reach_count[0, 0], jnp.float32).astype(jnp.bfloat16)
    payload = jnp.concatenate([cotangent.reshape(fields, cell_count)] + area_parts + [count_row], axis=0)
    payload = lax.optimization_barrier(payload)
    products = jnp.dot(
        payload[: fields + 3], jnp.concatenate(area_parts, axis=0).T, preferred_element_type=jnp.float32
    ).sum(axis=1)
    count = fields + 1
    stats = (
        products[:count]
        + jnp.pad(products[count : count + 1], (fields, 0))
        + jnp.pad(products[count + 1 : count + 2], (fields, 0))
    )
    stats, area_late = lax.optimization_barrier((stats, cell_area))
    stats = butterfly_sum(stats, ("lat", "lon"))
    factor = stats[:fields] / stats[fields]

    ring = [payload]
    for _ in range(slot_count // 2):
        ring.append(shifted(ring[-1], "lon", -2))
    odd = lax.axis_index("lon") % 2 == 1
    half = slot_count // 2
    offer = jnp.stack([jnp.where(odd, ring[k], ring[k + 1]) for k in range(half)])
    offer = lax.optimization_barrier(offer)
    swapped = lax.ppermute(offer, "lon", [(i, i ^ 1) for i in range(lax.axis_size("lon"))])
    pairs = jnp.stack([jnp.stack(ring[:half]), swapped], axis=1)
    stacked = pairs.reshape(slot_count, fields + 4, cell_count)
    counts = stacked[:, fields + 3, 0].astype(jnp.float32)
    live = counts > jnp.arange(slot_count, dtype=jnp.float32)
    stacked = jnp.where(live[:, None, None], stacked, jnp.zeros_like(stacked))
    flat = stacked.transpose(1, 0, 2).reshape(fields + 4, slot_count * cell_count)
    moments = jnp.dot(
        flat,
        weights[0, 0].reshape(slot_count * cell_count, 3 * cell_count),
        preferred_element_type=jnp.float32,
    )

    def block(moment_index, row):
        start = moment_index * cell_count + row * tile_cols
        return moments[:, start : start + tile_cols]

    mean_adj = jnp.stack([block(0, row) for row in range(tile_rows)], axis=1)
    curv_adj = jnp.stack([block(2, row) for row in range(tile_rows)], axis=1)
    sides = [
        jnp.stack([block(1, row) + sign * block(2, row) for row in range(tile_rows)], axis=1)
        for sign in (-3.0, 3.0)
    ]
    edge_pair = jnp.stack(sides, axis=1)
    padded = padded_2(edge_pair, (("lon", 3),), 2)
    left_pad = padded[:, 0]
    right_pad = padded[:, 1]
    near = (
        left_pad[..., 2 : tile_cols + 2]
        + left_pad[..., 1 : tile_cols + 1]
        - right_pad[..., 2 : tile_cols + 2]
        - right_pad[..., 3 : tile_cols + 3]
    )
    far = (
        left_pad[..., 3 : tile_cols + 3]
        + left_pad[..., 0:tile_cols]
        - right_pad[..., 4 : tile_cols + 4]
        - right_pad[..., 1 : tile_cols + 1]
    )
    stencil = mean_adj + 6.0 * curv_adj + 7.0 / 12.0 * near - 1.0 / 12.0 * far
    area_stencil = stencil[fields] + stencil[fields + 1] + stencil[fields + 2]
    return stencil[:fields] + factor[:, None, None] * (area_late[None] - area_stencil[None])


def solution(mesh):
    in_specs = (
        P(None, "lat", "lon"),
        P("lat", "lon"),
        P("lat", "lon"),
        P("lat", "lon", None, None, None),
    )
    out_specs = P(None, "lat", "lon")
    return jax.shard_map(
        on_device_body, mesh=mesh, in_specs=in_specs, out_specs=out_specs, check_vma=False
    )
```

```python
import jax
import jax.numpy as jnp
from jax import lax
from jax.sharding import PartitionSpec as P


def shifted(value, axis, by):
    length = lax.axis_size(axis)
    return lax.ppermute(value, axis, [(i, (i + by) % length) for i in range(length)])


def xor_rounds(length):
    rounds, step = [], 1
    while step < length:
        rounds.append([i ^ step for i in range(length)])
        step *= 2
    return rounds


def lat_rounds(length):
    if length != 16:
        return xor_rounds(length)
    def mirror(i, scale):
        digit = (i // scale) % 4
        return i + (3 - 2 * digit) * scale
    return [
        [i ^ 1 for i in range(length)],
        [mirror(i, 1) for i in range(length)],
        [i ^ 4 for i in range(length)],
        [mirror(i, 4) for i in range(length)],
    ]


def lon_rounds(length):
    if length != 32:
        return xor_rounds(length)
    def across(i):
        chip, core = divmod(i, 2)
        return 2 * ((chip + (12 if chip < 4 else 4 if chip < 8 else -4 if chip < 12 else -12)) % 16) + core
    return xor_rounds(length)[:4] + [[across(i) for i in range(length)]]


def butterfly_sum(value, axes):
    for axis in axes:
        length = lax.axis_size(axis)
        for partner_of in (lat_rounds if axis == "lat" else lon_rounds)(length):
            partner = lax.ppermute(value, axis, [(i, partner_of[i]) for i in range(length)])
            value = value + partner
    return value


def padded_2(block, sides, width):
    for axis, dim in sides:
        count = lax.axis_size(axis)
        forward = [(i, i + 1) for i in range(count - 1)]
        forward.append((count - 1, 0))
        backward = [(target, source) for source, target in forward]
        low = lax.ppermute(
            lax.slice_in_dim(block, block.shape[dim] - width, None, axis=dim), axis, forward
        )
        high = lax.ppermute(lax.slice_in_dim(block, 0, width, axis=dim), axis, backward)
        block = jnp.concatenate([low, block, high], axis=dim)
    return block


def split_bf16(value):
    high = lax.reduce_precision(value, exponent_bits=8, mantissa_bits=7)
    rest = value - high
    middle = lax.reduce_precision(rest, exponent_bits=8, mantissa_bits=7)
    low = rest - middle
    return [part.astype(jnp.bfloat16) for part in (high, middle, low)]


def on_device_body(cotangent, cell_area, reach_count, weights):
    fields, tile_rows, tile_cols = cotangent.shape
    cell_count = tile_rows * tile_cols
    slot_count = weights.shape[2]
    area_parts = split_bf16(cell_area.reshape(1, cell_count))
    count_row = jnp.full((1, cell_count), reach_count[0, 0], jnp.float32).astype(jnp.bfloat16)
    payload = jnp.concatenate([cotangent.reshape(fields, cell_count)] + area_parts + [count_row], axis=0)
    payload = lax.optimization_barrier(payload)
    products = jnp.dot(
        payload[: fields + 3], jnp.concatenate(area_parts, axis=0).T, preferred_element_type=jnp.float32
    ).sum(axis=1)
    stats, area_late = lax.optimization_barrier((products, cell_area))
    stats = butterfly_sum(stats, ("lat", "lon"))
    norm_sq = jnp.broadcast_to(stats[None, fields : fields + 3], (fields, 3)).sum(axis=1)
    factor = stats[:fields] / norm_sq

    ring = [payload]
    for _ in range(slot_count // 2):
        ring.append(shifted(ring[-1], "lon", -2))
    odd = lax.axis_index("lon") % 2 == 1
    half = slot_count // 2
    offer = jnp.stack([jnp.where(odd, ring[k], ring[k + 1]) for k in range(half)])
    offer = lax.optimization_barrier(offer)
    swapped = lax.ppermute(offer, "lon", [(i, i ^ 1) for i in range(lax.axis_size("lon"))])
    pairs = jnp.stack([jnp.stack(ring[:half]), swapped], axis=1)
    stacked = pairs.reshape(slot_count, fields + 4, cell_count)
    counts = stacked[:, fields + 3, 0].astype(jnp.float32)
    live = counts > jnp.arange(slot_count, dtype=jnp.float32)
    stacked = jnp.where(live[:, None, None], stacked, jnp.zeros_like(stacked))
    flat = stacked.transpose(1, 0, 2).reshape(fields + 4, slot_count * cell_count)
    moments = jnp.dot(
        flat,
        weights[0, 0].reshape(slot_count * cell_count, 3 * cell_count),
        preferred_element_type=jnp.float32,
    )

    def block(moment_index, row):
        start = moment_index * cell_count + row * tile_cols
        return moments[:, start : start + tile_cols]

    mean_adj = jnp.stack([block(0, row) for row in range(tile_rows)], axis=1)
    curv_adj = jnp.stack([block(2, row) for row in range(tile_rows)], axis=1)
    sides = [
        jnp.stack([block(1, row) + sign * block(2, row) for row in range(tile_rows)], axis=1)
        for sign in (-3.0, 3.0)
    ]
    edge_pair = jnp.stack(sides, axis=1)
    padded = padded_2(edge_pair, (("lon", 3),), 2)
    left_pad = padded[:, 0]
    right_pad = padded[:, 1]
    near = (
        left_pad[..., 2 : tile_cols + 2]
        + left_pad[..., 1 : tile_cols + 1]
        - right_pad[..., 2 : tile_cols + 2]
        - right_pad[..., 3 : tile_cols + 3]
    )
    far = (
        left_pad[..., 3 : tile_cols + 3]
        + left_pad[..., 0:tile_cols]
        - right_pad[..., 4 : tile_cols + 4]
        - right_pad[..., 1 : tile_cols + 1]
    )
    stencil = mean_adj + 6.0 * curv_adj + 7.0 / 12.0 * near - 1.0 / 12.0 * far
    area_stencil = stencil[fields] + stencil[fields + 1] + stencil[fields + 2]
    return stencil[:fields] + factor[:, None, None] * (area_late[None] - area_stencil[None])


def solution(mesh):
    in_specs = (
        P(None, "lat", "lon"),
        P("lat", "lon"),
        P("lat", "lon"),
        P("lat", "lon", None, None, None),
    )
    out_specs = P(None, "lat", "lon")
    return jax.shard_map(
        on_device_body, mesh=mesh, in_specs=in_specs, out_specs=out_specs, check_vma=False
    )
```
